256 devices in a mesh: rep: 16 (over z, core), wide: 4 (over x), narrow: 4 (over y).
Axes of the slice: x: 4, y: 4, z: 8, core: 2. Of those that a mesh axis runs over, the one named last changes fastest.
Arguments:
- tokens: bfloat16 [16384, 1536], P(('rep', 'wide'), 'narrow'), parts along dimension 0, may hold values from -6 to 6
- attn_gain: float32 [1536], replicated, may hold values from 0.1 to 1.9
- w_qkv: bfloat16 [1536, 2048], P(None, ('wide', 'narrow')), may hold values from -0.15625 to 0.15625
- w_out: bfloat16 [1536, 1536], P(None, 'narrow'), may hold values from -0.15625 to 0.15625
- prefix_cache: bfloat16 [2, 32, 8192, 2, 128], P(None, 'rep', ('wide', 'narrow')), parts along dimension 1, may hold values from -1500 to 1500
- decode_cache: bfloat16 [2, 64, 8192, 2, 128], P(None, 'rep', ('wide', 'narrow')), parts along dimension 1, may hold values from -1500 to 1500
- offsets: int32 [32], P('rep'), parts along dimension 0, may hold values from 1 to 8192, as said below
- lengths: int32 [64], P('rep'), parts along dimension 0, may hold values from 1 to 8192, as said below
Outputs:
- mixed: bfloat16 [16384, 1536], P(('rep', 'wide'), 'narrow'), parts along dimension 0
The draws below stay inside these ranges and needn't reach their ends.
There are 16 independent parts, one for each index of `rep`. The reference program is written for one: setup_inputs(seed, part) draws one part's arguments, and reference() takes and returns one part's arrays. A program takes and returns all parts, laid end to end along the dimension named above; an argument that names none is the same for every part. Nothing has to cross between parts.
Inputs may be any that keep to these rules, and one draw needn't show every extreme that they name: `offsets`: exactly one prefill block has 8192 cached positions. `lengths`: exactly one decode has 8192 cached positions.
All inputs are finite; a program needn't handle non-finite values.
Results may differ from the reference program's by a relative error of at most 0.008.
Values may be sent and summed in bfloat16 or wider, within the bound.
No kernel may reach another device: no remote copies, remote signals or barrier semaphores. Data moves between devices by JAX's collectives and lax.ppermute only.
A program may use at most 320 MiB of HBM per device.

```python
import jax
import jax.numpy as jnp
from jax import lax

D = 1536
QUERY_HEADS = 12
KEY_VALUE_HEADS = 2
HEAD_SIZE = 128
SPAN = 510
PREFILL_BLOCKS = 2
DECODE_REQUESTS = 4
CACHE_LENGTH = 8192
TOKEN_ROWS = 1024
QKVW = 2048


def cache_entry(key, shape):
    base = jnp.clip(jax.random.normal(key, shape, jnp.float32), -6.0, 6.0)
    return base.astype(jnp.bfloat16)


def limits(key, count):
    first, second = jax.random.split(key)
    values = jax.random.randint(first, (count,), 1, 3 * CACHE_LENGTH // 4 + 1)
    which = jax.random.randint(second, (), 0, count)
    return jnp.where(jnp.arange(count) == which, CACHE_LENGTH, values).astype(jnp.int32)


def draw_prefix_cache(key, part):
    return cache_entry(key, (2, PREFILL_BLOCKS, CACHE_LENGTH, KEY_VALUE_HEADS, HEAD_SIZE))


def draw_decode_cache(key, part):
    return cache_entry(key, (2, DECODE_REQUESTS, CACHE_LENGTH, KEY_VALUE_HEADS, HEAD_SIZE))


def draw_offsets(key, part):
    return limits(key, PREFILL_BLOCKS)


def draw_lengths(key, part):
    return limits(key, DECODE_REQUESTS)


def steps_of(rng, extent, cuts, smallest, high):
    factor_of = 1.0
    for axis_at, parts in cuts:
        draws = jax.random.uniform(jax.random.fold_in(jax.random.fold_in(rng, 6), axis_at), (parts,), jnp.float32, smallest / len(cuts), high / len(cuts))
        factor_of = factor_of * jnp.repeat(jnp.exp(draws), extent[axis_at] // parts).reshape((-1,) + (1,) * (len(extent) - 1 - axis_at))
    return factor_of


def normal_values(own_key, extent, scale, reach, pieces=(), kind=jnp.bfloat16):
    factor_of = steps_of(own_key, extent, pieces, -0.22, 0.18) if pieces else 1.0
    array = jax.random.normal(own_key, extent, jnp.float32) * scale * factor_of
    return jnp.minimum(jnp.maximum(array, -reach), reach).astype(kind)


def setup_inputs(seed: int = 0, part: int = 0) -> dict:
    seeds = jax.random.split(jax.random.key(seed), 9)
    part_keys = jax.random.split(jax.random.fold_in(seeds[8], part), 9)
    return {
        "tokens": normal_values(part_keys[0], (TOKEN_ROWS, D), 1.0, 6.0, ((0, 4), (1, 4))),
        "attn_gain": jnp.clip(1.0 + 0.18 * jax.random.normal(seeds[1], (D,), jnp.float32), 0.1, 1.9),
        "w_qkv": normal_values(seeds[2], (D, QKVW), D ** -0.5, 0.15625, ((1, 16),)),
        "w_out": normal_values(seeds[3], (QUERY_HEADS * HEAD_SIZE, D), (QUERY_HEADS * HEAD_SIZE) ** -0.5, 0.15625, ((1, 4),)),
        "prefix_cache": draw_prefix_cache(jax.random.fold_in(jax.random.fold_in(seeds[8], part), 71), part),
        "decode_cache": draw_decode_cache(jax.random.fold_in(jax.random.fold_in(seeds[8], part), 71), part),
        "offsets": draw_offsets(jax.random.fold_in(jax.random.fold_in(seeds[8], part), 71), part),
        "lengths": draw_lengths(jax.random.fold_in(jax.random.fold_in(seeds[8], part), 71), part),
    }


EPS = 1e-06
NEG = -1e+30

def attend(grouped_queries, keys, values, allowed, form_s, form_o):
    scores = jnp.einsum(form_s, grouped_queries.astype(jnp.float32), keys.astype(jnp.float32)) * grouped_queries.shape[-1] ** (-0.5)
    masked = jnp.where(allowed, scores, NEG)
    peak = lax.optimization_barrier(jnp.max(masked, -1))
    weights = jnp.where(allowed, jnp.exp(masked - peak[..., None]), 0.0)
    total = lax.optimization_barrier(jnp.sum(weights, -1))
    rounded = weights.astype(jnp.bfloat16).astype(jnp.float32)
    weighted = jnp.einsum(form_o, rounded, values.astype(jnp.float32))
    return weighted / total[..., None]

def reference(tokens, attn_gain, w_qkv, w_out, prefix_cache, decode_cache, offsets, lengths):
    full = tokens.astype(jnp.float32)
    meansq = lax.optimization_barrier(jnp.mean(full * full, -1, keepdims=True))
    normed = (full * lax.rsqrt(meansq + EPS) * attn_gain).astype(jnp.bfloat16)
    query_key_value = jnp.dot(normed, w_qkv, preferred_element_type=jnp.float32).astype(jnp.bfloat16)
    query_width = QUERY_HEADS * HEAD_SIZE
    query_matrix = query_key_value[:, :query_width].reshape(TOKEN_ROWS, QUERY_HEADS, HEAD_SIZE)
    incoming_keys = query_key_value[:, query_width:query_width + KEY_VALUE_HEADS * HEAD_SIZE].reshape(TOKEN_ROWS, KEY_VALUE_HEADS, HEAD_SIZE)
    incoming_values = query_key_value[:, query_width + KEY_VALUE_HEADS * HEAD_SIZE:].reshape(TOKEN_ROWS, KEY_VALUE_HEADS, HEAD_SIZE)
    grouped_queries = query_matrix.reshape(TOKEN_ROWS, KEY_VALUE_HEADS, QUERY_HEADS // KEY_VALUE_HEADS, HEAD_SIZE)
    outputs = []
    places = jnp.arange(CACHE_LENGTH, dtype=jnp.int32)
    steps = jnp.arange(SPAN, dtype=jnp.int32)
    for index in range(PREFILL_BLOCKS):
        lo = index * SPAN
        keys = jnp.concatenate([prefix_cache[0, index], incoming_keys[lo:lo + SPAN]], 0)
        vals = jnp.concatenate([prefix_cache[1, index], incoming_values[lo:lo + SPAN]], 0)
        cached = jnp.broadcast_to((places < offsets[index])[None, :], (SPAN, CACHE_LENGTH))
        fresh = steps[None, :] <= steps[:, None]
        allowed = jnp.concatenate([cached, fresh], 1)[:, None, None, :]
        outputs.append(attend(grouped_queries[lo:lo + SPAN], keys, vals, allowed, 'qhgd,khd->qhgk', 'qhgk,khd->qhgd'))
    lo = PREFILL_BLOCKS * SPAN
    keys = jnp.concatenate([decode_cache[0], incoming_keys[lo:][:, None]], 1)
    vals = jnp.concatenate([decode_cache[1], incoming_values[lo:][:, None]], 1)
    cached = places[None, :] < lengths[:, None]
    allowed = jnp.concatenate([cached, jnp.ones((DECODE_REQUESTS, 1), dtype=bool)], 1)[:, None, None, :]
    outputs.append(attend(grouped_queries[lo:], keys, vals, allowed, 'nhgd,nkhd->nhgk', 'nhgk,nkhd->nhgd'))
    attended = jnp.concatenate(outputs, 0).astype(jnp.bfloat16).reshape(TOKEN_ROWS, query_width)
    mixed = full + jnp.dot(attended, w_out, preferred_element_type=jnp.float32)
    return mixed.astype(jnp.bfloat16)
```

```python
import jax
import jax.numpy as jnp
from jax import lax
from jax.sharding import PartitionSpec as P

EPS = 1e-06
NEG = -1e30


def normalize(rows, gain):
    full = rows.astype(jnp.float32)
    meansq = jnp.mean(full * full, -1, keepdims=True)
    return (full * lax.rsqrt(meansq + EPS) * gain).astype(jnp.bfloat16)


def partial_softmax(grouped_queries, keys, values, allowed, form_s, form_o):
    scores = jnp.einsum(
        form_s, grouped_queries, keys, preferred_element_type=jnp.float32
    ) * grouped_queries.shape[-1] ** (-0.5)
    masked = jnp.where(allowed, scores, NEG)
    peak = jnp.max(masked, -1)
    weights = jnp.where(allowed, jnp.exp(masked - peak[..., None]), 0.0)
    total = jnp.sum(weights, -1)
    weighted = jnp.einsum(
        form_o, weights.astype(jnp.bfloat16), values, preferred_element_type=jnp.float32
    )
    return (peak, total, weighted)


def join_parts(first, second):
    peak = jnp.maximum(first[0], second[0])
    scale_a = jnp.exp(first[0] - peak)
    scale_b = jnp.exp(second[0] - peak)
    total = first[1] * scale_a + second[1] * scale_b
    weighted = first[2] * scale_a[..., None] + second[2] * scale_b[..., None]
    return (peak, total, weighted)


def per_device(tokens, attn_gain, w_qkv, w_out, prefix_cache, decode_cache, offsets, lengths):
    n_wide = lax.axis_size("wide")
    n_narrow = lax.axis_size("narrow")
    devices = n_wide * n_narrow
    joined = lax.axis_index("wide") * n_narrow + lax.axis_index("narrow")
    block_rows = tokens.shape[0]
    every_rows = block_rows * n_wide
    own = every_rows // devices
    head_dim = prefix_cache.shape[-1]
    kv_heads = prefix_cache.shape[-2]
    n_prefix = prefix_cache.shape[1]
    n_decode = decode_cache.shape[1]
    span = (every_rows - n_decode) // n_prefix
    q_width = w_out.shape[0]
    heads = q_width // head_dim
    group = heads // kv_heads
    starts = (offsets[:, None] + jnp.arange(span, dtype=jnp.int32)[None, :]).reshape(-1)
    positions = jnp.concatenate([starts, lengths])
    row_ids = jnp.arange(every_rows, dtype=jnp.int32)
    sequence = jnp.where(
        row_ids < n_prefix * span, row_ids // span, row_ids - n_prefix * span + n_prefix
    )
    own_start = joined * own
    own_pos = lax.dynamic_slice_in_dim(positions, own_start, own)
    own_seq = lax.dynamic_slice_in_dim(sequence, own_start, own)
    features = lax.all_gather(tokens, "narrow", axis=1, tiled=True)
    everyone = lax.all_gather(features, "wide", axis=0, tiled=True)
    normed_rows = normalize(everyone, attn_gain)
    columns = jnp.dot(normed_rows, w_qkv, preferred_element_type=jnp.float32).astype(jnp.bfloat16)
    qkv_all = lax.all_gather(columns, ("wide", "narrow"), axis=1, tiled=True)
    query_matrix = qkv_all[:, :q_width].reshape(every_rows, heads, head_dim)
    own_qkv = lax.dynamic_slice_in_dim(qkv_all, own_start, own, 0)
    kv_width = kv_heads * head_dim
    own_keys = own_qkv[:, q_width : q_width + kv_width].reshape(own, kv_heads, head_dim)
    own_values = own_qkv[:, q_width + kv_width :].reshape(own, kv_heads, head_dim)
    grouped_queries = query_matrix.reshape(every_rows, kv_heads, group, head_dim)
    shard = prefix_cache.shape[2]
    cache_pos = joined * shard + jnp.arange(shard, dtype=jnp.int32)
    pieces = []
    for index in range(n_prefix):
        block = grouped_queries[index * span : (index + 1) * span]
        allowed = (cache_pos < offsets[index])[None, None, None, :]
        pieces.append(
            partial_softmax(
                block,
                prefix_cache[0, index],
                prefix_cache[1, index],
                allowed,
                "qhgd,khd->qhgk",
                "qhgk,khd->qhgd",
            )
        )
    allowed = (cache_pos[None, :] < lengths[:, None])[:, None, None, :]
    pieces.append(
        partial_softmax(
            grouped_queries[n_prefix * span :],
            decode_cache[0],
            decode_cache[1],
            allowed,
            "nhgd,nkhd->nhgk",
            "nhgk,nkhd->nhgd",
        )
    )
    cached = tuple((jnp.concatenate([piece[slot] for piece in pieces], 0) for slot in range(3)))
    allowed = ((sequence[:, None] == own_seq[None, :]) & (own_pos[None, :] <= positions[:, None]))[
        :, None, None, :
    ]
    fresh = partial_softmax(
        grouped_queries, own_keys, own_values, allowed, "rhgd,khd->rhgk", "rhgk,khd->rhgd"
    )
    peak, total, weighted = join_parts(cached, fresh)
    axes = ("wide", "narrow")
    top = lax.pmax(peak, axes)
    scale = jnp.exp(peak - top)
    total = lax.psum_scatter(total * scale, axes, scatter_dimension=0, tiled=True)
    weighted = lax.psum_scatter(
        weighted * scale[..., None], axes, scatter_dimension=0, tiled=True
    )
    attended = (weighted / total[..., None]).astype(jnp.bfloat16).reshape(own, q_width)
    mine_rows = lax.all_gather(attended, "narrow", axis=0, tiled=True)
    mixed = tokens.astype(jnp.float32) + jnp.dot(
        mine_rows, w_out, preferred_element_type=jnp.float32
    )
    return mixed.astype(jnp.bfloat16)


def solution(mesh):
    return jax.shard_map(
        per_device,
        mesh=mesh,
        in_specs=(
            P(("rep", "wide"), "narrow"),
            P(),
            P(None, ("wide", "narrow")),
            P(None, "narrow"),
            P(None, "rep", ("wide", "narrow"), None, None),
            P(None, "rep", ("wide", "narrow"), None, None),
            P("rep"),
            P("rep"),
        ),
        out_specs=P(("rep", "wide"), "narrow"),
        check_vma=False,
    )
```

```python
import jax
import jax.numpy as jnp
from jax import lax
from jax.sharding import PartitionSpec as P

EPS = 1e-06
NEG = -1e30


def normalize(rows, gain):
    full = rows.astype(jnp.float32)
    meansq = jnp.mean(full * full, -1, keepdims=True)
    return (full * lax.rsqrt(meansq + EPS) * gain).astype(jnp.bfloat16)


def partial_softmax(grouped_queries, keys, values, allowed, form_s, form_o):
    scores = jnp.einsum(
        form_s, grouped_queries, keys, preferred_element_type=jnp.float32
    ) * grouped_queries.shape[-1] ** (-0.5)
    masked = jnp.where(allowed, scores, NEG)
    peak = jnp.max(masked, -1)
    weights = jnp.where(allowed, jnp.exp(masked - peak[..., None]), 0.0)
    total = jnp.sum(weights, -1)
    weighted = jnp.einsum(
        form_o, weights.astype(jnp.bfloat16), values, preferred_element_type=jnp.float32
    )
    return (peak, total, weighted)


def join_parts(first, second):
    peak = jnp.maximum(first[0], second[0])
    scale_a = jnp.exp(first[0] - peak)
    scale_b = jnp.exp(second[0] - peak)
    total = first[1] * scale_a + second[1] * scale_b
    weighted = first[2] * scale_a[..., None] + second[2] * scale_b[..., None]
    return (peak, total, weighted)


def per_device(tokens, attn_gain, w_qkv, w_out, prefix_cache, decode_cache, offsets, lengths):
    n_wide = lax.axis_size("wide")
    n_narrow = lax.axis_size("narrow")
    devices = n_wide * n_narrow
    joined = lax.axis_index("wide") * n_narrow + lax.axis_index("narrow")
    block_rows = tokens.shape[0]
    every_rows = block_rows * n_wide
    own = every_rows // devices
    head_dim = prefix_cache.shape[-1]
    kv_heads = prefix_cache.shape[-2]
    n_prefix = prefix_cache.shape[1]
    n_decode = decode_cache.shape[1]
    span = (every_rows - n_decode) // n_prefix
    q_width = w_out.shape[0]
    heads = q_width // head_dim
    group = heads // kv_heads
    starts = (offsets[:, None] + jnp.arange(span, dtype=jnp.int32)[None, :]).reshape(-1)
    positions = jnp.concatenate([starts, lengths])
    row_ids = jnp.arange(every_rows, dtype=jnp.int32)
    sequence = jnp.where(
        row_ids < n_prefix * span, row_ids // span, row_ids - n_prefix * span + n_prefix
    )
    own_start = joined * own
    own_pos = lax.dynamic_slice_in_dim(positions, own_start, own)
    own_seq = lax.dynamic_slice_in_dim(sequence, own_start, own)
    features = lax.all_gather(tokens, "narrow", axis=1, tiled=True)
    everyone = lax.all_gather(features, "wide", axis=0, tiled=True)
    normed_rows = normalize(everyone, attn_gain)
    columns = jnp.dot(normed_rows, w_qkv, preferred_element_type=jnp.float32).astype(jnp.bfloat16)
    qkv_all = lax.all_gather(columns, ("wide", "narrow"), axis=1, tiled=True)
    query_matrix = qkv_all[:, :q_width].reshape(every_rows, heads, head_dim)
    own_qkv = lax.dynamic_slice_in_dim(qkv_all, own_start, own, 0)
    kv_width = kv_heads * head_dim
    own_keys = own_qkv[:, q_width : q_width + kv_width].reshape(own, kv_heads, head_dim)
    own_values = own_qkv[:, q_width + kv_width :].reshape(own, kv_heads, head_dim)
    grouped_queries = query_matrix.reshape(every_rows, kv_heads, group, head_dim)
    shard = prefix_cache.shape[2]
    cache_pos = joined * shard + jnp.arange(shard, dtype=jnp.int32)
    pieces = []
    for index in range(n_prefix):
        block = grouped_queries[index * span : (index + 1) * span]
        allowed = (cache_pos < offsets[index])[None, None, None, :]
        pieces.append(
            partial_softmax(
                block,
                prefix_cache[0, index],
                prefix_cache[1, index],
                allowed,
                "qhgd,khd->qhgk",
                "qhgk,khd->qhgd",
            )
        )
    allowed = (cache_pos[None, :] < lengths[:, None])[:, None, None, :]
    pieces.append(
        partial_softmax(
            grouped_queries[n_prefix * span :],
            decode_cache[0],
            decode_cache[1],
            allowed,
            "nhgd,nkhd->nhgk",
            "nhgk,nkhd->nhgd",
        )
    )
    cached = tuple((jnp.concatenate([piece[slot] for piece in pieces], 0) for slot in range(3)))
    allowed = ((sequence[:, None] == own_seq[None, :]) & (own_pos[None, :] <= positions[:, None]))[
        :, None, None, :
    ]
    fresh = partial_softmax(
        grouped_queries, own_keys, own_values, allowed, "rhgd,khd->rhgk", "rhgk,khd->rhgd"
    )
    peak, total, weighted = join_parts(cached, fresh)
    top = lax.pmax(lax.pmax(peak, "narrow"), "wide")
    scale = jnp.exp(peak - top)
    lanes = 128
    packed = jnp.concatenate(
        [
            (weighted * scale[..., None]).reshape(every_rows, q_width),
            (total * scale).reshape(every_rows, heads),
            jnp.zeros((every_rows, lanes - heads), jnp.float32),
        ],
        1,
    )
    width = packed.shape[1]
    packed = (
        packed.astype(jnp.bfloat16)
        .reshape(n_wide, n_narrow, own, width)
        .transpose(1, 0, 2, 3)
        .reshape(every_rows, width)
    )
    packed = lax.psum_scatter(packed, "narrow", scatter_dimension=0, tiled=True)
    packed = lax.psum_scatter(packed, "wide", scatter_dimension=0, tiled=True)
    packed = packed.astype(jnp.float32)
    total = packed[:, q_width : q_width + heads].reshape(own, heads, 1)
    weighted = packed[:, :q_width].reshape(own, heads, head_dim)
    attended = (weighted / total).astype(jnp.bfloat16).reshape(own, q_width)
    mine_rows = lax.all_gather(attended, "narrow", axis=0, tiled=True)
    mixed = tokens.astype(jnp.float32) + jnp.dot(
        mine_rows, w_out, preferred_element_type=jnp.float32
    )
    return mixed.astype(jnp.bfloat16)


def solution(mesh):
    return jax.shard_map(
        per_device,
        mesh=mesh,
        in_specs=(
            P(("rep", "wide"), "narrow"),
            P(),
            P(None, ("wide", "narrow")),
            P(None, "narrow"),
            P(None, "rep", ("wide", "narrow"), None, None),
            P(None, "rep", ("wide", "narrow"), None, None),
            P("rep"),
            P("rep"),
        ),
        out_specs=P(("rep", "wide"), "narrow"),
        check_vma=False,
    )
```

```python
import jax
import jax.numpy as jnp
from jax import lax
from jax.sharding import PartitionSpec as P

EPS = 1e-06
NEG = -1e30


def normalize(rows, gain):
    full = rows.astype(jnp.float32)
    meansq = jnp.mean(full * full, -1, keepdims=True)
    return (full * lax.rsqrt(meansq + EPS) * gain).astype(jnp.bfloat16)


def partial_softmax(grouped_queries, keys, values, allowed, form_s, form_o):
    scores = jnp.einsum(
        form_s, grouped_queries, keys, preferred_element_type=jnp.float32
    ) * grouped_queries.shape[-1] ** (-0.5)
    masked = jnp.where(allowed, scores, NEG)
    peak = jnp.max(masked, -1)
    weights = jnp.where(allowed, jnp.exp(masked - peak[..., None]), 0.0)
    total = jnp.sum(weights, -1)
    weighted = jnp.einsum(
        form_o, weights.astype(jnp.bfloat16), values, preferred_element_type=jnp.float32
    )
    return (peak, total, weighted)


def join_parts(first, second):
    peak = jnp.maximum(first[0], second[0])
    scale_a = jnp.exp(first[0] - peak)
    scale_b = jnp.exp(second[0] - peak)
    total = first[1] * scale_a + second[1] * scale_b
    weighted = first[2] * scale_a[..., None] + second[2] * scale_b[..., None]
    return (peak, total, weighted)


def per_device(tokens, attn_gain, w_qkv, w_out, prefix_cache, decode_cache, offsets, lengths):
    n_wide = lax.axis_size("wide")
    n_narrow = lax.axis_size("narrow")
    devices = n_wide * n_narrow
    joined = lax.axis_index("wide") * n_narrow + lax.axis_index("narrow")
    block_rows = tokens.shape[0]
    every_rows = block_rows * n_wide
    own = every_rows // devices
    head_dim = prefix_cache.shape[-1]
    kv_heads = prefix_cache.shape[-2]
    n_prefix = prefix_cache.shape[1]
    n_decode = decode_cache.shape[1]
    span = (every_rows - n_decode) // n_prefix
    q_width = w_out.shape[0]
    heads = q_width // head_dim
    group = heads // kv_heads
    starts = (offsets[:, None] + jnp.arange(span, dtype=jnp.int32)[None, :]).reshape(-1)
    positions = jnp.concatenate([starts, lengths])
    row_ids = jnp.arange(every_rows, dtype=jnp.int32)
    sequence = jnp.where(
        row_ids < n_prefix * span, row_ids // span, row_ids - n_prefix * span + n_prefix
    )
    own_start = joined * own
    own_pos = lax.dynamic_slice_in_dim(positions, own_start, own)
    own_seq = lax.dynamic_slice_in_dim(sequence, own_start, own)
    features = lax.all_gather(tokens, "narrow", axis=1, tiled=True)
    normed_rows = normalize(features, attn_gain)
    w_cols = lax.all_gather(w_qkv, "wide", axis=0, tiled=False)
    part = jnp.einsum(
        "rf,wfc->rwc", normed_rows, w_cols, preferred_element_type=jnp.float32
    ).astype(jnp.bfloat16)
    col_block = w_qkv.shape[1]
    part = part.reshape(block_rows, n_wide * col_block)
    gathered = lax.all_gather(part, ("wide", "narrow"), axis=0, tiled=False)
    qkv_all = (
        gathered.reshape(n_wide, n_narrow, block_rows, n_wide, col_block)
        .transpose(0, 2, 3, 1, 4)
        .reshape(every_rows, devices * col_block)
    )
    query_matrix = qkv_all[:, :q_width].reshape(every_rows, heads, head_dim)
    own_qkv = lax.dynamic_slice_in_dim(qkv_all, own_start, own, 0)
    kv_width = kv_heads * head_dim
    own_keys = own_qkv[:, q_width : q_width + kv_width].reshape(own, kv_heads, head_dim)
    own_values = own_qkv[:, q_width + kv_width :].reshape(own, kv_heads, head_dim)
    grouped_queries = query_matrix.reshape(every_rows, kv_heads, group, head_dim)
    shard = prefix_cache.shape[2]
    cache_pos = joined * shard + jnp.arange(shard, dtype=jnp.int32)
    pieces = []
    for index in range(n_prefix):
        block = grouped_queries[index * span : (index + 1) * span]
        allowed = (cache_pos < offsets[index])[None, None, None, :]
        pieces.append(
            partial_softmax(
                block,
                prefix_cache[0, index],
                prefix_cache[1, index],
                allowed,
                "qhgd,khd->qhgk",
                "qhgk,khd->qhgd",
            )
        )
    allowed = (cache_pos[None, :] < lengths[:, None])[:, None, None, :]
    pieces.append(
        partial_softmax(
            grouped_queries[n_prefix * span :],
            decode_cache[0],
            decode_cache[1],
            allowed,
            "nhgd,nkhd->nhgk",
            "nhgk,nkhd->nhgd",
        )
    )
    cached = tuple((jnp.concatenate([piece[slot] for piece in pieces], 0) for slot in range(3)))
    allowed = ((sequence[:, None] == own_seq[None, :]) & (own_pos[None, :] <= positions[:, None]))[
        :, None, None, :
    ]
    fresh = partial_softmax(
        grouped_queries, own_keys, own_values, allowed, "rhgd,khd->rhgk", "rhgk,khd->rhgd"
    )
    peak, total, weighted = join_parts(cached, fresh)
    top = lax.pmax(lax.pmax(peak, "narrow"), "wide")
    scale = jnp.exp(peak - top)
    lanes = 128
    packed = jnp.concatenate(
        [
            (weighted * scale[..., None]).reshape(every_rows, q_width),
            (total * scale).reshape(every_rows, heads),
            jnp.zeros((every_rows, lanes - heads), jnp.float32),
        ],
        1,
    )
    width = packed.shape[1]
    packed = (
        packed.astype(jnp.bfloat16)
        .reshape(n_wide, n_narrow, own, width)
        .transpose(1, 0, 2, 3)
        .reshape(every_rows, width)
    )
    packed = lax.psum_scatter(packed, "narrow", scatter_dimension=0, tiled=True)
    packed = lax.psum_scatter(packed, "wide", scatter_dimension=0, tiled=True)
    packed = packed.astype(jnp.float32)
    total = packed[:, q_width : q_width + heads].reshape(own, heads, 1)
    weighted = packed[:, :q_width].reshape(own, heads, head_dim)
    attended = (weighted / total).astype(jnp.bfloat16).reshape(own, q_width)
    mine_rows = lax.all_gather(attended, "narrow", axis=0, tiled=True)
    mixed = tokens.astype(jnp.float32) + jnp.dot(
        mine_rows, w_out, preferred_element_type=jnp.float32
    )
    return mixed.astype(jnp.bfloat16)


def solution(mesh):
    return jax.shard_map(
        per_device,
        mesh=mesh,
        in_specs=(
            P(("rep", "wide"), "narrow"),
            P(),
            P(None, ("wide", "narrow")),
            P(None, "narrow"),
            P(None, "rep", ("wide", "narrow"), None, None),
            P(None, "rep", ("wide", "narrow"), None, None),
            P("rep"),
            P("rep"),
        ),
        out_specs=P(("rep", "wide"), "narrow"),
        check_vma=False,
    )
```

```python
import jax
import jax.numpy as jnp
from jax import lax
from jax.sharding import PartitionSpec as P

EPS = 1e-06
NEG = -1e30


def normalize(rows, gain):
    full = rows.astype(jnp.float32)
    meansq = jnp.mean(full * full, -1, keepdims=True)
    return (full * lax.rsqrt(meansq + EPS) * gain).astype(jnp.bfloat16)


def partial_softmax(grouped_queries, keys, values, allowed, form_s, form_o):
    scores = jnp.einsum(
        form_s, grouped_queries, keys, preferred_element_type=jnp.float32
    ) * grouped_queries.shape[-1] ** (-0.5)
    masked = jnp.where(allowed, scores, NEG)
    peak = jnp.max(masked, -1)
    weights = jnp.where(allowed, jnp.exp(masked - peak[..., None]), 0.0)
    total = jnp.sum(weights, -1)
    weighted = jnp.einsum(
        form_o, weights.astype(jnp.bfloat16), values, preferred_element_type=jnp.float32
    )
    return (peak, total, weighted)


def join_parts(first, second):
    peak = jnp.maximum(first[0], second[0])
    scale_a = jnp.exp(first[0] - peak)
    scale_b = jnp.exp(second[0] - peak)
    total = first[1] * scale_a + second[1] * scale_b
    weighted = first[2] * scale_a[..., None] + second[2] * scale_b[..., None]
    return (peak, total, weighted)


def per_device(tokens, attn_gain, w_qkv, w_out, prefix_cache, decode_cache, offsets, lengths):
    n_wide = lax.axis_size("wide")
    n_narrow = lax.axis_size("narrow")
    devices = n_wide * n_narrow
    joined = lax.axis_index("wide") * n_narrow + lax.axis_index("narrow")
    block_rows = tokens.shape[0]
    every_rows = block_rows * n_wide
    own = every_rows // devices
    head_dim = prefix_cache.shape[-1]
    kv_heads = prefix_cache.shape[-2]
    n_prefix = prefix_cache.shape[1]
    n_decode = decode_cache.shape[1]
    span = (every_rows - n_decode) // n_prefix
    q_width = w_out.shape[0]
    heads = q_width // head_dim
    group = heads // kv_heads
    starts = (offsets[:, None] + jnp.arange(span, dtype=jnp.int32)[None, :]).reshape(-1)
    positions = jnp.concatenate([starts, lengths])
    row_ids = jnp.arange(every_rows, dtype=jnp.int32)
    sequence = jnp.where(
        row_ids < n_prefix * span, row_ids // span, row_ids - n_prefix * span + n_prefix
    )
    own_start = joined * own
    own_pos = lax.dynamic_slice_in_dim(positions, own_start, own)
    own_seq = lax.dynamic_slice_in_dim(sequence, own_start, own)
    features = lax.all_gather(tokens, "narrow", axis=1, tiled=True)
    normed_rows = normalize(features, attn_gain)
    w_cols = lax.all_gather(w_qkv, "wide", axis=0, tiled=False)
    part = jnp.einsum(
        "rf,wfc->rwc", normed_rows, w_cols, preferred_element_type=jnp.float32
    ).astype(jnp.bfloat16)
    col_block = w_qkv.shape[1]
    part = part.reshape(block_rows, n_wide * col_block)
    gathered = lax.all_gather(part, ("wide", "narrow"), axis=0, tiled=False)
    qkv_all = (
        gathered.reshape(n_wide, n_narrow, block_rows, n_wide, col_block)
        .transpose(0, 2, 3, 1, 4)
        .reshape(every_rows, devices * col_block)
    )
    query_matrix = qkv_all[:, :q_width].reshape(every_rows, heads, head_dim)
    own_qkv = lax.dynamic_slice_in_dim(qkv_all, own_start, own, 0)
    kv_width = kv_heads * head_dim
    own_keys = own_qkv[:, q_width : q_width + kv_width].reshape(own, kv_heads, head_dim)
    own_values = own_qkv[:, q_width + kv_width :].reshape(own, kv_heads, head_dim)
    grouped_queries = query_matrix.reshape(every_rows, kv_heads, group, head_dim)
    shard = prefix_cache.shape[2]
    cache_pos = joined * shard + jnp.arange(shard, dtype=jnp.int32)
    pieces = []
    for index in range(n_prefix):
        block = grouped_queries[index * span : (index + 1) * span]
        allowed = (cache_pos < offsets[index])[None, None, None, :]
        pieces.append(
            partial_softmax(
                block,
                prefix_cache[0, index],
                prefix_cache[1, index],
                allowed,
                "qhgd,khd->qhgk",
                "qhgk,khd->qhgd",
            )
        )
    allowed = (cache_pos[None, :] < lengths[:, None])[:, None, None, :]
    pieces.append(
        partial_softmax(
            grouped_queries[n_prefix * span :],
            decode_cache[0],
            decode_cache[1],
            allowed,
            "nhgd,nkhd->nhgk",
            "nhgk,nkhd->nhgd",
        )
    )
    cached = tuple((jnp.concatenate([piece[slot] for piece in pieces], 0) for slot in range(3)))
    allowed = ((sequence[:, None] == own_seq[None, :]) & (own_pos[None, :] <= positions[:, None]))[
        :, None, None, :
    ]
    fresh = partial_softmax(
        grouped_queries, own_keys, own_values, allowed, "rhgd,khd->rhgk", "rhgk,khd->rhgd"
    )
    peak, total, weighted = join_parts(cached, fresh)
    top = lax.pmax(lax.pmax(peak, "narrow"), "wide")
    scale = jnp.exp(peak - top)
    lanes = 128
    packed = jnp.concatenate(
        [
            (weighted * scale[..., None]).reshape(every_rows, q_width),
            (total * scale).reshape(every_rows, heads),
            jnp.zeros((every_rows, lanes - heads), jnp.float32),
        ],
        1,
    )
    width = packed.shape[1]
    packed = (
        packed.astype(jnp.bfloat16)
        .reshape(n_wide, n_narrow, own, width)
        .transpose(1, 0, 2, 3)
        .reshape(every_rows, width)
    )
    packed = lax.psum_scatter(packed, "narrow", scatter_dimension=0, tiled=True)
    packed = lax.all_to_all(packed.reshape(n_wide, own, width), "wide", 0, 0)
    packed = jnp.sum(packed.astype(jnp.float32), 0)
    total = packed[:, q_width : q_width + heads].reshape(own, heads, 1)
    weighted = packed[:, :q_width].reshape(own, heads, head_dim)
    attended = (weighted / total).astype(jnp.bfloat16).reshape(own, q_width)
    mine_rows = lax.all_gather(attended, "narrow", axis=0, tiled=True)
    mixed = tokens.astype(jnp.float32) + jnp.dot(
        mine_rows, w_out, preferred_element_type=jnp.float32
    )
    return mixed.astype(jnp.bfloat16)


def solution(mesh):
    return jax.shard_map(
        per_device,
        mesh=mesh,
        in_specs=(
            P(("rep", "wide"), "narrow"),
            P(),
            P(None, ("wide", "narrow")),
            P(None, "narrow"),
            P(None, "rep", ("wide", "narrow"), None, None),
            P(None, "rep", ("wide", "narrow"), None, None),
            P("rep"),
            P("rep"),
        ),
        out_specs=P(("rep", "wide"), "narrow"),
        check_vma=False,
    )
```

```python
import jax
import jax.numpy as jnp
from jax import lax
from jax.sharding import PartitionSpec as P

EPS = 1e-06
NEG = -1e30


def normalize(rows, gain):
    full = rows.astype(jnp.float32)
    meansq = jnp.mean(full * full, -1, keepdims=True)
    return (full * lax.rsqrt(meansq + EPS) * gain).astype(jnp.bfloat16)


def partial_softmax(grouped_queries, keys, values, allowed, form_s, form_o):
    scores = jnp.einsum(
        form_s, grouped_queries, keys, preferred_element_type=jnp.float32
    ) * grouped_queries.shape[-1] ** (-0.5)
    masked = jnp.where(allowed, scores, NEG)
    peak = jnp.max(masked, -1)
    weights = jnp.where(allowed, jnp.exp(masked - peak[..., None]), 0.0)
    total = jnp.sum(weights, -1)
    weighted = jnp.einsum(
        form_o, weights.astype(jnp.bfloat16), values, preferred_element_type=jnp.float32
    )
    return (peak, total, weighted)


def join_parts(first, second):
    peak = jnp.maximum(first[0], second[0])
    scale_a = jnp.exp(first[0] - peak)
    scale_b = jnp.exp(second[0] - peak)
    total = first[1] * scale_a + second[1] * scale_b
    weighted = first[2] * scale_a[..., None] + second[2] * scale_b[..., None]
    return (peak, total, weighted)


def per_device(tokens, attn_gain, w_qkv, w_out, prefix_cache, decode_cache, offsets, lengths):
    n_wide = lax.axis_size("wide")
    n_narrow = lax.axis_size("narrow")
    devices = n_wide * n_narrow
    joined = lax.axis_index("wide") * n_narrow + lax.axis_index("narrow")
    block_rows = tokens.shape[0]
    every_rows = block_rows * n_wide
    own = every_rows // devices
    head_dim = prefix_cache.shape[-1]
    kv_heads = prefix_cache.shape[-2]
    n_prefix = prefix_cache.shape[1]
    n_decode = decode_cache.shape[1]
    span = (every_rows - n_decode) // n_prefix
    q_width = w_out.shape[0]
    heads = q_width // head_dim
    group = heads // kv_heads
    starts = (offsets[:, None] + jnp.arange(span, dtype=jnp.int32)[None, :]).reshape(-1)
    positions = jnp.concatenate([starts, lengths])
    row_ids = jnp.arange(every_rows, dtype=jnp.int32)
    sequence = jnp.where(
        row_ids < n_prefix * span, row_ids // span, row_ids - n_prefix * span + n_prefix
    )
    own_start = joined * own
    own_pos = lax.dynamic_slice_in_dim(positions, own_start, own)
    own_seq = lax.dynamic_slice_in_dim(sequence, own_start, own)
    features = lax.all_gather(tokens, "narrow", axis=1, tiled=True)
    normed_rows = normalize(features, attn_gain)
    w_cols = lax.all_gather(w_qkv, "wide", axis=0, tiled=False)
    part = jnp.einsum(
        "rf,wfc->rwc", normed_rows, w_cols, preferred_element_type=jnp.float32
    ).astype(jnp.bfloat16)
    col_block = w_qkv.shape[1]
    part = part.reshape(block_rows, n_wide * col_block)
    gathered = lax.all_gather(part, ("wide", "narrow"), axis=0, tiled=False)
    qkv_all = (
        gathered.reshape(n_wide, n_narrow, block_rows, n_wide, col_block)
        .transpose(0, 2, 3, 1, 4)
        .reshape(every_rows, devices * col_block)
    )
    query_matrix = qkv_all[:, :q_width].reshape(every_rows, heads, head_dim)
    own_qkv = lax.dynamic_slice_in_dim(qkv_all, own_start, own, 0)
    kv_width = kv_heads * head_dim
    own_keys = own_qkv[:, q_width : q_width + kv_width].reshape(own, kv_heads, head_dim)
    own_values = own_qkv[:, q_width + kv_width :].reshape(own, kv_heads, head_dim)
    grouped_queries = query_matrix.reshape(every_rows, kv_heads, group, head_dim)
    shard = prefix_cache.shape[2]
    cache_pos = joined * shard + jnp.arange(shard, dtype=jnp.int32)
    pieces = []
    for index in range(n_prefix):
        block = grouped_queries[index * span : (index + 1) * span]
        allowed = (cache_pos < offsets[index])[None, None, None, :]
        pieces.append(
            partial_softmax(
                block,
                prefix_cache[0, index],
                prefix_cache[1, index],
                allowed,
                "qhgd,khd->qhgk",
                "qhgk,khd->qhgd",
            )
        )
    allowed = (cache_pos[None, :] < lengths[:, None])[:, None, None, :]
    pieces.append(
        partial_softmax(
            grouped_queries[n_prefix * span :],
            decode_cache[0],
            decode_cache[1],
            allowed,
            "nhgd,nkhd->nhgk",
            "nhgk,nkhd->nhgd",
        )
    )
    cached = tuple((jnp.concatenate([piece[slot] for piece in pieces], 0) for slot in range(3)))
    allowed = ((sequence[:, None] == own_seq[None, :]) & (own_pos[None, :] <= positions[:, None]))[
        :, None, None, :
    ]
    fresh = partial_softmax(
        grouped_queries, own_keys, own_values, allowed, "rhgd,khd->rhgk", "rhgk,khd->rhgd"
    )
    peak, total, weighted = join_parts(cached, fresh)
    top = lax.pmax(peak, "narrow")
    hi = lax.reduce_precision(top, exponent_bits=8, mantissa_bits=7)
    lo = lax.reduce_precision(top - hi, exponent_bits=8, mantissa_bits=7)
    shift = hi + lo
    scale = jnp.exp(jnp.minimum(peak - shift, 80.0))
    first = lax.axis_index("narrow") == 0

    def kept(a):
        return jnp.where(first, a, jnp.zeros_like(a)).reshape(every_rows, heads)

    lanes = 128
    packed = jnp.concatenate(
        [
            (weighted * scale[..., None]).reshape(every_rows, q_width),
            (total * scale).reshape(every_rows, heads),
            kept(hi),
            kept(lo),
            jnp.zeros((every_rows, lanes - 3 * heads), jnp.float32),
        ],
        1,
    )
    width = packed.shape[1]
    packed = (
        packed.astype(jnp.bfloat16)
        .reshape(n_wide, n_narrow, own, width)
        .transpose(1, 0, 2, 3)
        .reshape(every_rows, width)
    )
    packed = lax.psum_scatter(packed, "narrow", scatter_dimension=0, tiled=True)
    packed = lax.all_to_all(packed.reshape(n_wide, own, width), "wide", 0, 0)
    packed = packed.astype(jnp.float32)
    part_shift = (
        packed[:, :, q_width + heads : q_width + 2 * heads]
        + packed[:, :, q_width + 2 * heads : q_width + 3 * heads]
    )
    part_scale = jnp.exp(part_shift - jnp.max(part_shift, 0)[None])
    total = jnp.sum(packed[:, :, q_width : q_width + heads] * part_scale, 0)
    total = total.reshape(own, heads, 1)
    weighted = packed[:, :, :q_width].reshape(n_wide, own, heads, head_dim)
    weighted = jnp.sum(weighted * part_scale[..., None], 0)
    attended = (weighted / total).astype(jnp.bfloat16).reshape(own, q_width)
    mine_rows = lax.all_gather(attended, "narrow", axis=0, tiled=True)
    mixed = tokens.astype(jnp.float32) + jnp.dot(
        mine_rows, w_out, preferred_element_type=jnp.float32
    )
    return mixed.astype(jnp.bfloat16)


def solution(mesh):
    return jax.shard_map(
        per_device,
        mesh=mesh,
        in_specs=(
            P(("rep", "wide"), "narrow"),
            P(),
            P(None, ("wide", "narrow")),
            P(None, "narrow"),
            P(None, "rep", ("wide", "narrow"), None, None),
            P(None, "rep", ("wide", "narrow"), None, None),
            P("rep"),
            P("rep"),
        ),
        out_specs=P(("rep", "wide"), "narrow"),
        check_vma=False,
    )
```

```python
import jax
import jax.numpy as jnp
from jax import lax
from jax.sharding import PartitionSpec as P

EPS = 1e-06
NEG = -1e30


def normalize(rows, gain):
    full = rows.astype(jnp.float32)
    meansq = jnp.mean(full * full, -1, keepdims=True)
    return (full * lax.rsqrt(meansq + EPS) * gain).astype(jnp.bfloat16)


def masked_scores(grouped_queries, keys, allowed, form_s):
    scores = jnp.einsum(
        form_s, grouped_queries, keys, preferred_element_type=jnp.float32
    ) * grouped_queries.shape[-1] ** (-0.5)
    return jnp.where(allowed, scores, NEG)


def weigh(masked, allowed, shift, values, form_o):
    weights = jnp.where(allowed, jnp.exp(jnp.minimum(masked - shift[..., None], 80.0)), 0.0)
    total = jnp.sum(weights, -1)
    weighted = jnp.einsum(
        form_o, weights.astype(jnp.bfloat16), values, preferred_element_type=jnp.float32
    )
    return total, weighted


def per_device(tokens, attn_gain, w_qkv, w_out, prefix_cache, decode_cache, offsets, lengths):
    n_wide = lax.axis_size("wide")
    n_narrow = lax.axis_size("narrow")
    devices = n_wide * n_narrow
    joined = lax.axis_index("wide") * n_narrow + lax.axis_index("narrow")
    block_rows = tokens.shape[0]
    every_rows = block_rows * n_wide
    own = every_rows // devices
    head_dim = prefix_cache.shape[-1]
    kv_heads = prefix_cache.shape[-2]
    n_prefix = prefix_cache.shape[1]
    n_decode = decode_cache.shape[1]
    span = (every_rows - n_decode) // n_prefix
    q_width = w_out.shape[0]
    heads = q_width // head_dim
    group = heads // kv_heads
    starts = (offsets[:, None] + jnp.arange(span, dtype=jnp.int32)[None, :]).reshape(-1)
    positions = jnp.concatenate([starts, lengths])
    row_ids = jnp.arange(every_rows, dtype=jnp.int32)
    sequence = jnp.where(
        row_ids < n_prefix * span, row_ids // span, row_ids - n_prefix * span + n_prefix
    )
    own_start = joined * own
    own_pos = lax.dynamic_slice_in_dim(positions, own_start, own)
    own_seq = lax.dynamic_slice_in_dim(sequence, own_start, own)
    features = lax.all_gather(tokens, "narrow", axis=1, tiled=True)
    normed_rows = normalize(features, attn_gain)
    w_cols = lax.all_gather(w_qkv, "wide", axis=0, tiled=False)
    part = jnp.einsum(
        "rf,wfc->rwc", normed_rows, w_cols, preferred_element_type=jnp.float32
    ).astype(jnp.bfloat16)
    col_block = w_qkv.shape[1]
    part = part.reshape(block_rows, n_wide * col_block)
    gathered = lax.all_gather(part, ("wide", "narrow"), axis=0, tiled=False)
    qkv_all = (
        gathered.reshape(n_wide, n_narrow, block_rows, n_wide, col_block)
        .transpose(0, 2, 3, 1, 4)
        .reshape(every_rows, devices * col_block)
    )
    query_matrix = qkv_all[:, :q_width].reshape(every_rows, heads, head_dim)
    own_qkv = lax.dynamic_slice_in_dim(qkv_all, own_start, own, 0)
    kv_width = kv_heads * head_dim
    own_keys = own_qkv[:, q_width : q_width + kv_width].reshape(own, kv_heads, head_dim)
    own_values = own_qkv[:, q_width + kv_width :].reshape(own, kv_heads, head_dim)
    grouped_queries = query_matrix.reshape(every_rows, kv_heads, group, head_dim)
    shard = prefix_cache.shape[2]
    cache_pos = joined * shard + jnp.arange(shard, dtype=jnp.int32)
    pieces = []
    for index in range(n_prefix):
        rows = slice(index * span, (index + 1) * span)
        allowed = (cache_pos < offsets[index])[None, None, None, :]
        pieces.append(
            (
                rows,
                masked_scores(grouped_queries[rows], prefix_cache[0, index], allowed, "qhgd,khd->qhgk"),
                allowed,
                prefix_cache[1, index],
                "qhgk,khd->qhgd",
            )
        )
    rows = slice(n_prefix * span, every_rows)
    allowed = (cache_pos[None, :] < lengths[:, None])[:, None, None, :]
    pieces.append(
        (
            rows,
            masked_scores(grouped_queries[rows], decode_cache[0], allowed, "nhgd,nkhd->nhgk"),
            allowed,
            decode_cache[1],
            "nhgk,nkhd->nhgd",
        )
    )
    allowed = ((sequence[:, None] == own_seq[None, :]) & (own_pos[None, :] <= positions[:, None]))[
        :, None, None, :
    ]
    fresh = masked_scores(grouped_queries, own_keys, allowed, "rhgd,khd->rhgk")
    peak = jnp.concatenate([jnp.max(piece[1], -1) for piece in pieces], 0)
    peak = jnp.maximum(peak, jnp.max(fresh, -1))
    top = lax.pmax(peak, "narrow")
    hi = lax.reduce_precision(top, exponent_bits=8, mantissa_bits=7)
    lo = lax.reduce_precision(top - hi, exponent_bits=8, mantissa_bits=7)
    shift = hi + lo
    total, weighted = weigh(fresh, allowed, shift, own_values, "rhgk,khd->rhgd")
    cached = [weigh(m, ok, shift[rows], v, form) for rows, m, ok, v, form in pieces]
    total = total + jnp.concatenate([piece[0] for piece in cached], 0)
    weighted = weighted + jnp.concatenate([piece[1] for piece in cached], 0)
    first = lax.axis_index("narrow") == 0

    def kept(a):
        return jnp.where(first, a, jnp.zeros_like(a)).reshape(every_rows, heads)

    lanes = 128
    packed = jnp.concatenate(
        [
            weighted.reshape(every_rows, q_width),
            total.reshape(every_rows, heads),
            kept(hi),
            kept(lo),
            jnp.zeros((every_rows, lanes - 3 * heads), jnp.float32),
        ],
        1,
    )
    width = packed.shape[1]
    packed = (
        packed.astype(jnp.bfloat16)
        .reshape(n_wide, n_narrow, own, width)
        .transpose(1, 0, 2, 3)
        .reshape(every_rows, width)
    )
    packed = lax.psum_scatter(packed, "narrow", scatter_dimension=0, tiled=True)
    packed = lax.all_to_all(packed.reshape(n_wide, own, width), "wide", 0, 0)
    packed = packed.astype(jnp.float32)
    part_shift = (
        packed[:, :, q_width + heads : q_width + 2 * heads]
        + packed[:, :, q_width + 2 * heads : q_width + 3 * heads]
    )
    part_scale = jnp.exp(part_shift - jnp.max(part_shift, 0)[None])
    total = jnp.sum(packed[:, :, q_width : q_width + heads] * part_scale, 0)
    total = total.reshape(own, heads, 1)
    weighted = packed[:, :, :q_width].reshape(n_wide, own, heads, head_dim)
    weighted = jnp.sum(weighted * part_scale[..., None], 0)
    attended = (weighted / total).astype(jnp.bfloat16).reshape(own, q_width)
    mine_rows = lax.all_gather(attended, "narrow", axis=0, tiled=True)
    mixed = tokens.astype(jnp.float32) + jnp.dot(
        mine_rows, w_out, preferred_element_type=jnp.float32
    )
    return mixed.astype(jnp.bfloat16)


def solution(mesh):
    return jax.shard_map(
        per_device,
        mesh=mesh,
        in_specs=(
            P(("rep", "wide"), "narrow"),
            P(),
            P(None, ("wide", "narrow")),
            P(None, "narrow"),
            P(None, "rep", ("wide", "narrow"), None, None),
            P(None, "rep", ("wide", "narrow"), None, None),
            P("rep"),
            P("rep"),
        ),
        out_specs=P(("rep", "wide"), "narrow"),
        check_vma=False,
    )
```

```python
import jax
import jax.numpy as jnp
from jax import lax
from jax.sharding import PartitionSpec as P

EPS = 1e-06
NEG = -1e30


def normalize(rows, gain):
    full = rows.astype(jnp.float32)
    meansq = jnp.mean(full * full, -1, keepdims=True)
    return (full * lax.rsqrt(meansq + EPS) * gain).astype(jnp.bfloat16)


def partial_softmax(grouped_queries, keys, values, allowed, form_s, form_o):
    scores = jnp.einsum(
        form_s, grouped_queries, keys, preferred_element_type=jnp.float32
    ) * grouped_queries.shape[-1] ** (-0.5)
    masked = jnp.where(allowed, scores, NEG)
    peak = jnp.max(masked, -1)
    weights = jnp.where(allowed, jnp.exp(masked - peak[..., None]), 0.0)
    total = jnp.sum(weights, -1)
    weighted = jnp.einsum(
        form_o, weights.astype(jnp.bfloat16), values, preferred_element_type=jnp.float32
    )
    return (peak, total, weighted)


def join_parts(first, second):
    peak = jnp.maximum(first[0], second[0])
    scale_a = jnp.exp(first[0] - peak)
    scale_b = jnp.exp(second[0] - peak)
    total = first[1] * scale_a + second[1] * scale_b
    weighted = first[2] * scale_a[..., None] + second[2] * scale_b[..., None]
    return (peak, total, weighted)


def per_device(tokens, attn_gain, w_qkv, w_out, prefix_cache, decode_cache, offsets, lengths):
    n_wide = lax.axis_size("wide")
    n_narrow = lax.axis_size("narrow")
    devices = n_wide * n_narrow
    joined = lax.axis_index("wide") * n_narrow + lax.axis_index("narrow")
    block_rows = tokens.shape[0]
    every_rows = block_rows * n_wide
    own = every_rows // devices
    head_dim = prefix_cache.shape[-1]
    kv_heads = prefix_cache.shape[-2]
    n_prefix = prefix_cache.shape[1]
    n_decode = decode_cache.shape[1]
    span = (every_rows - n_decode) // n_prefix
    q_width = w_out.shape[0]
    heads = q_width // head_dim
    group = heads // kv_heads
    starts = (offsets[:, None] + jnp.arange(span, dtype=jnp.int32)[None, :]).reshape(-1)
    positions = jnp.concatenate([starts, lengths])
    row_ids = jnp.arange(every_rows, dtype=jnp.int32)
    sequence = jnp.where(
        row_ids < n_prefix * span, row_ids // span, row_ids - n_prefix * span + n_prefix
    )
    own_start = joined * own
    own_pos = lax.dynamic_slice_in_dim(positions, own_start, own)
    own_seq = lax.dynamic_slice_in_dim(sequence, own_start, own)
    features = lax.all_gather(tokens, "narrow", axis=1, tiled=True)
    normed_rows = normalize(features, attn_gain)
    w_cols = lax.all_gather(w_qkv, "wide", axis=0, tiled=False)
    part = jnp.einsum(
        "rf,wfc->rwc", normed_rows, w_cols, preferred_element_type=jnp.float32
    ).astype(jnp.bfloat16)
    col_block = w_qkv.shape[1]
    q_blocks = q_width // (n_narrow * col_block)
    gathered = lax.all_gather(part[:, :q_blocks], ("wide", "narrow"), axis=0, tiled=False)
    query_matrix = (
        gathered.reshape(n_wide, n_narrow, block_rows, q_blocks, col_block)
        .transpose(0, 2, 3, 1, 4)
        .reshape(every_rows, heads, head_dim)
    )
    fresh_kv = part[:, q_blocks:].reshape(n_narrow, own, col_block)
    fresh_kv = lax.all_to_all(fresh_kv, "narrow", 0, 0)
    own_keys = fresh_kv[:kv_heads].transpose(1, 0, 2)
    own_values = fresh_kv[kv_heads:].transpose(1, 0, 2)
    grouped_queries = query_matrix.reshape(every_rows, kv_heads, group, head_dim)
    shard = prefix_cache.shape[2]
    cache_pos = joined * shard + jnp.arange(shard, dtype=jnp.int32)
    pieces = []
    for index in range(n_prefix):
        block = grouped_queries[index * span : (index + 1) * span]
        allowed = (cache_pos < offsets[index])[None, None, None, :]
        pieces.append(
            partial_softmax(
                block,
                prefix_cache[0, index],
                prefix_cache[1, index],
                allowed,
                "qhgd,khd->qhgk",
                "qhgk,khd->qhgd",
            )
        )
    allowed = (cache_pos[None, :] < lengths[:, None])[:, None, None, :]
    pieces.append(
        partial_softmax(
            grouped_queries[n_prefix * span :],
            decode_cache[0],
            decode_cache[1],
            allowed,
            "nhgd,nkhd->nhgk",
            "nhgk,nkhd->nhgd",
        )
    )
    cached = tuple((jnp.concatenate([piece[slot] for piece in pieces], 0) for slot in range(3)))
    allowed = ((sequence[:, None] == own_seq[None, :]) & (own_pos[None, :] <= positions[:, None]))[
        :, None, None, :
    ]
    fresh = partial_softmax(
        grouped_queries, own_keys, own_values, allowed, "rhgd,khd->rhgk", "rhgk,khd->rhgd"
    )
    peak, total, weighted = join_parts(cached, fresh)
    top = lax.pmax(peak, "narrow")
    hi = lax.reduce_precision(top, exponent_bits=8, mantissa_bits=7)
    lo = lax.reduce_precision(top - hi, exponent_bits=8, mantissa_bits=7)
    shift = hi + lo
    scale = jnp.exp(jnp.minimum(peak - shift, 80.0))
    first = lax.axis_index("narrow") == 0

    def kept(a):
        return jnp.where(first, a, jnp.zeros_like(a)).reshape(every_rows, heads)

    lanes = 128
    packed = jnp.concatenate(
        [
            (weighted * scale[..., None]).reshape(every_rows, q_width),
            (total * scale).reshape(every_rows, heads),
            kept(hi),
            kept(lo),
            jnp.zeros((every_rows, lanes - 3 * heads), jnp.float32),
        ],
        1,
    )
    width = packed.shape[1]
    packed = (
        packed.astype(jnp.bfloat16)
        .reshape(n_wide, n_narrow, own, width)
        .transpose(1, 0, 2, 3)
        .reshape(every_rows, width)
    )
    packed = lax.psum_scatter(packed, "narrow", scatter_dimension=0, tiled=True)
    packed = lax.all_to_all(packed.reshape(n_wide, own, width), "wide", 0, 0)
    packed = packed.astype(jnp.float32)
    part_shift = (
        packed[:, :, q_width + heads : q_width + 2 * heads]
        + packed[:, :, q_width + 2 * heads : q_width + 3 * heads]
    )
    part_scale = jnp.exp(part_shift - jnp.max(part_shift, 0)[None])
    total = jnp.sum(packed[:, :, q_width : q_width + heads] * part_scale, 0)
    total = total.reshape(own, heads, 1)
    weighted = packed[:, :, :q_width].reshape(n_wide, own, heads, head_dim)
    weighted = jnp.sum(weighted * part_scale[..., None], 0)
    attended = (weighted / total).astype(jnp.bfloat16).reshape(own, q_width)
    mine_rows = lax.all_gather(attended, "narrow", axis=0, tiled=True)
    mixed = tokens.astype(jnp.float32) + jnp.dot(
        mine_rows, w_out, preferred_element_type=jnp.float32
    )
    return mixed.astype(jnp.bfloat16)


def solution(mesh):
    return jax.shard_map(
        per_device,
        mesh=mesh,
        in_specs=(
            P(("rep", "wide"), "narrow"),
            P(),
            P(None, ("wide", "narrow")),
            P(None, "narrow"),
            P(None, "rep", ("wide", "narrow"), None, None),
            P(None, "rep", ("wide", "narrow"), None, None),
            P("rep"),
            P("rep"),
        ),
        out_specs=P(("rep", "wide"), "narrow"),
        check_vma=False,
    )
```

```python
import jax
import jax.numpy as jnp
from jax import lax
from jax.sharding import PartitionSpec as P

EPS = 1e-06
NEG = -1e30


def normalize(rows, gain):
    full = rows.astype(jnp.float32)
    meansq = jnp.mean(full * full, -1, keepdims=True)
    return (full * lax.rsqrt(meansq + EPS) * gain).astype(jnp.bfloat16)


def partial_softmax(grouped_queries, keys, values, allowed, form_s, form_o):
    scores = jnp.einsum(
        form_s, grouped_queries, keys, preferred_element_type=jnp.float32
    ) * grouped_queries.shape[-1] ** (-0.5)
    masked = jnp.where(allowed, scores, NEG)
    peak = jnp.max(masked, -1)
    weights = jnp.where(allowed, jnp.exp(masked - peak[..., None]), 0.0)
    total = jnp.sum(weights, -1)
    weighted = jnp.einsum(
        form_o, weights.astype(jnp.bfloat16), values, preferred_element_type=jnp.float32
    )
    return (peak, total, weighted)


def join_parts(first, second):
    peak = jnp.maximum(first[0], second[0])
    scale_a = jnp.exp(first[0] - peak)
    scale_b = jnp.exp(second[0] - peak)
    total = first[1] * scale_a + second[1] * scale_b
    weighted = first[2] * heads_major(scale_a) + second[2] * heads_major(scale_b)
    return (peak, total, weighted)


def heads_major(scale):
    return scale.transpose(1, 2, 0)[..., None]


def per_device(tokens, attn_gain, w_qkv, w_out, prefix_cache, decode_cache, offsets, lengths):
    n_wide = lax.axis_size("wide")
    n_narrow = lax.axis_size("narrow")
    devices = n_wide * n_narrow
    joined = lax.axis_index("wide") * n_narrow + lax.axis_index("narrow")
    block_rows = tokens.shape[0]
    every_rows = block_rows * n_wide
    own = every_rows // devices
    head_dim = prefix_cache.shape[-1]
    kv_heads = prefix_cache.shape[-2]
    n_prefix = prefix_cache.shape[1]
    n_decode = decode_cache.shape[1]
    span = (every_rows - n_decode) // n_prefix
    q_width = w_out.shape[0]
    heads = q_width // head_dim
    group = heads // kv_heads
    starts = (offsets[:, None] + jnp.arange(span, dtype=jnp.int32)[None, :]).reshape(-1)
    positions = jnp.concatenate([starts, lengths])
    row_ids = jnp.arange(every_rows, dtype=jnp.int32)
    sequence = jnp.where(
        row_ids < n_prefix * span, row_ids // span, row_ids - n_prefix * span + n_prefix
    )
    own_start = joined * own
    own_pos = lax.dynamic_slice_in_dim(positions, own_start, own)
    own_seq = lax.dynamic_slice_in_dim(sequence, own_start, own)
    features = lax.all_gather(tokens, "narrow", axis=1, tiled=True)
    normed_rows = normalize(features, attn_gain)
    w_cols = lax.all_gather(w_qkv, "wide", axis=0, tiled=False)
    part = jnp.einsum(
        "rf,wfc->rwc", normed_rows, w_cols, preferred_element_type=jnp.float32
    ).astype(jnp.bfloat16)
    col_block = w_qkv.shape[1]
    q_blocks = q_width // (n_narrow * col_block)
    gathered = lax.all_gather(part[:, :q_blocks], ("wide", "narrow"), axis=0, tiled=False)
    query_matrix = (
        gathered.reshape(n_wide, n_narrow, block_rows, q_blocks, col_block)
        .transpose(0, 2, 3, 1, 4)
        .reshape(every_rows, heads, head_dim)
    )
    fresh_kv = part[:, q_blocks:].reshape(n_narrow, own, col_block)
    fresh_kv = lax.all_to_all(fresh_kv, "narrow", 0, 0)
    own_keys = fresh_kv[:kv_heads].transpose(1, 0, 2)
    own_values = fresh_kv[kv_heads:].transpose(1, 0, 2)
    grouped_queries = query_matrix.reshape(every_rows, kv_heads, group, head_dim)
    shard = prefix_cache.shape[2]
    cache_pos = joined * shard + jnp.arange(shard, dtype=jnp.int32)
    pieces = []
    for index in range(n_prefix):
        block = grouped_queries[index * span : (index + 1) * span]
        allowed = (cache_pos < offsets[index])[None, None, None, :]
        pieces.append(
            partial_softmax(
                block,
                prefix_cache[0, index],
                prefix_cache[1, index],
                allowed,
                "qhgd,khd->qhgk",
                "qhgk,khd->hgqd",
            )
        )
    allowed = (cache_pos[None, :] < lengths[:, None])[:, None, None, :]
    pieces.append(
        partial_softmax(
            grouped_queries[n_prefix * span :],
            decode_cache[0],
            decode_cache[1],
            allowed,
            "nhgd,nkhd->nhgk",
            "nhgk,nkhd->hgnd",
        )
    )
    cached = tuple((jnp.concatenate([piece[slot] for piece in pieces], 2 * (slot // 2)) for slot in range(3)))
    allowed = ((sequence[:, None] == own_seq[None, :]) & (own_pos[None, :] <= positions[:, None]))[
        :, None, None, :
    ]
    fresh = partial_softmax(
        grouped_queries, own_keys, own_values, allowed, "rhgd,khd->rhgk", "rhgk,khd->hgrd"
    )
    peak, total, weighted = join_parts(cached, fresh)
    top = lax.pmax(peak, "narrow")
    hi = lax.reduce_precision(top, exponent_bits=8, mantissa_bits=7)
    lo = lax.reduce_precision(top - hi, exponent_bits=8, mantissa_bits=7)
    shift = hi + lo
    scale = jnp.exp(jnp.minimum(peak - shift, 80.0))
    first = lax.axis_index("narrow") == 0

    def kept(a):
        return jnp.where(first, a, jnp.zeros_like(a)).reshape(every_rows, heads)

    lanes = 128
    extra = jnp.concatenate(
        [
            (total * scale).reshape(every_rows, heads),
            kept(hi),
            kept(lo),
            jnp.zeros((every_rows, lanes - 3 * heads), jnp.float32),
        ],
        1,
    )
    scaled = (weighted * heads_major(scale)).reshape(heads, every_rows, head_dim)
    packed = jnp.concatenate([scaled, extra[None]], 0).astype(jnp.bfloat16)
    slots = packed.shape[0]
    packed = (
        packed.reshape(slots, n_wide, n_narrow, own, head_dim)
        .transpose(0, 2, 1, 3, 4)
        .reshape(slots, every_rows, head_dim)
    )
    packed = lax.psum_scatter(packed, "narrow", scatter_dimension=1, tiled=True)
    packed = lax.all_to_all(packed.reshape(slots, n_wide, own, head_dim), "wide", 1, 1)
    packed = packed.astype(jnp.float32)
    extra = packed[heads]
    part_shift = extra[..., heads : 2 * heads] + extra[..., 2 * heads : 3 * heads]
    part_scale = jnp.exp(part_shift - jnp.max(part_shift, 0)[None])
    total = jnp.sum(extra[..., :heads] * part_scale, 0)
    weighted = jnp.sum(packed[:heads] * part_scale.transpose(2, 0, 1)[..., None], 1)
    attended = weighted / total.T[..., None]
    attended = attended.astype(jnp.bfloat16).transpose(1, 0, 2).reshape(own, q_width)
    mine_rows = lax.all_gather(attended, "narrow", axis=0, tiled=True)
    mixed = tokens.astype(jnp.float32) + jnp.dot(
        mine_rows, w_out, preferred_element_type=jnp.float32
    )
    return mixed.astype(jnp.bfloat16)


def solution(mesh):
    return jax.shard_map(
        per_device,
        mesh=mesh,
        in_specs=(
            P(("rep", "wide"), "narrow"),
            P(),
            P(None, ("wide", "narrow")),
            P(None, "narrow"),
            P(None, "rep", ("wide", "narrow"), None, None),
            P(None, "rep", ("wide", "narrow"), None, None),
            P("rep"),
            P("rep"),
        ),
        out_specs=P(("rep", "wide"), "narrow"),
        check_vma=False,
    )
```

```python
import jax
import jax.numpy as jnp
from jax import lax
from jax.sharding import PartitionSpec as P

EPS = 1e-06
NEG = -1e30


def normalize(rows, gain):
    full = rows.astype(jnp.float32)
    meansq = jnp.mean(full * full, -1, keepdims=True)
    return (full * lax.rsqrt(meansq + EPS) * gain).astype(jnp.bfloat16)


def partial_softmax(grouped_queries, keys, values, allowed, form_s, form_o):
    scores = jnp.einsum(
        form_s, grouped_queries, keys, preferred_element_type=jnp.float32
    ) * grouped_queries.shape[-1] ** (-0.5)
    masked = jnp.where(allowed, scores, NEG)
    peak = jnp.max(masked, -1)
    weights = jnp.where(allowed, jnp.exp(masked - peak[..., None]), 0.0)
    total = jnp.sum(weights, -1)
    weighted = jnp.einsum(
        form_o, weights.astype(jnp.bfloat16), values, preferred_element_type=jnp.float32
    )
    return (peak, total, weighted)


def join_parts(first, second):
    peak = jnp.maximum(first[0], second[0])
    scale_a = jnp.exp(first[0] - peak)
    scale_b = jnp.exp(second[0] - peak)
    total = first[1] * scale_a + second[1] * scale_b
    weighted = first[2] * heads_major(scale_a) + second[2] * heads_major(scale_b)
    return (peak, total, weighted)


def heads_major(scale):
    return scale.transpose(1, 2, 0)[..., None]


def per_device(tokens, attn_gain, w_qkv, w_out, prefix_cache, decode_cache, offsets, lengths):
    n_wide = lax.axis_size("wide")
    n_narrow = lax.axis_size("narrow")
    devices = n_wide * n_narrow
    joined = lax.axis_index("wide") * n_narrow + lax.axis_index("narrow")
    block_rows = tokens.shape[0]
    every_rows = block_rows * n_wide
    own = every_rows // devices
    head_dim = prefix_cache.shape[-1]
    kv_heads = prefix_cache.shape[-2]
    n_prefix = prefix_cache.shape[1]
    n_decode = decode_cache.shape[1]
    span = (every_rows - n_decode) // n_prefix
    q_width = w_out.shape[0]
    heads = q_width // head_dim
    group = heads // kv_heads
    starts = (offsets[:, None] + jnp.arange(span, dtype=jnp.int32)[None, :]).reshape(-1)
    positions = jnp.concatenate([starts, lengths])
    row_ids = jnp.arange(every_rows, dtype=jnp.int32)
    sequence = jnp.where(
        row_ids < n_prefix * span, row_ids // span, row_ids - n_prefix * span + n_prefix
    )
    own_start = joined * own
    own_pos = lax.dynamic_slice_in_dim(positions, own_start, own)
    own_seq = lax.dynamic_slice_in_dim(sequence, own_start, own)
    features = lax.all_gather(tokens, "narrow", axis=1, tiled=True)
    normed_rows = normalize(features, attn_gain)
    w_cols = lax.all_gather(w_qkv, "wide", axis=0, tiled=False)
    part = jnp.einsum(
        "rf,wfc->rwc", normed_rows, w_cols, preferred_element_type=jnp.float32
    ).astype(jnp.bfloat16)
    col_block = w_qkv.shape[1]
    q_blocks = q_width // (n_narrow * col_block)
    gathered = lax.all_gather(part[:, :q_blocks], ("wide", "narrow"), axis=0, tiled=False)
    query_matrix = (
        gathered.reshape(n_wide, n_narrow, block_rows, q_blocks, col_block)
        .transpose(0, 2, 3, 1, 4)
        .reshape(every_rows, heads, head_dim)
    )
    fresh_kv = part[:, q_blocks:].reshape(n_narrow, own, col_block)
    fresh_kv = lax.all_to_all(fresh_kv, "narrow", 0, 0)
    own_keys = fresh_kv[:kv_heads].transpose(1, 0, 2)
    own_values = fresh_kv[kv_heads:].transpose(1, 0, 2)
    grouped_queries = query_matrix.reshape(every_rows, kv_heads, group, head_dim)
    shard = prefix_cache.shape[2]
    cache_pos = joined * shard + jnp.arange(shard, dtype=jnp.int32)
    pieces = []
    for index in range(n_prefix):
        block = grouped_queries[index * span : (index + 1) * span]
        allowed = (cache_pos < offsets[index])[None, None, None, :]
        pieces.append(
            partial_softmax(
                block,
                prefix_cache[0, index],
                prefix_cache[1, index],
                allowed,
                "qhgd,khd->qhgk",
                "qhgk,khd->hgqd",
            )
        )
    allowed = (cache_pos[None, :] < lengths[:, None])[:, None, None, :]
    pieces.append(
        partial_softmax(
            grouped_queries[n_prefix * span :],
            decode_cache[0],
            decode_cache[1],
            allowed,
            "nhgd,nkhd->nhgk",
            "nhgk,nkhd->hgnd",
        )
    )
    cached = tuple((jnp.concatenate([piece[slot] for piece in pieces], 2 * (slot // 2)) for slot in range(3)))
    allowed = ((sequence[:, None] == own_seq[None, :]) & (own_pos[None, :] <= positions[:, None]))[
        :, None, None, :
    ]
    fresh = partial_softmax(
        grouped_queries, own_keys, own_values, allowed, "rhgd,khd->rhgk", "rhgk,khd->hgrd"
    )
    top = lax.pmax(jnp.maximum(cached[0], fresh[0]), "narrow")
    hi = lax.reduce_precision(top, exponent_bits=8, mantissa_bits=7)
    lo = lax.reduce_precision(top - hi, exponent_bits=8, mantissa_bits=7)
    shift = hi + lo
    scale_a = jnp.exp(jnp.minimum(cached[0] - shift, 80.0))
    scale_b = jnp.exp(jnp.minimum(fresh[0] - shift, 80.0))
    total = cached[1] * scale_a + fresh[1] * scale_b
    weighted = cached[2] * heads_major(scale_a) + fresh[2] * heads_major(scale_b)
    first = lax.axis_index("narrow") == 0

    def kept(a):
        return jnp.where(first, a, jnp.zeros_like(a)).reshape(every_rows, heads)

    lanes = 128
    extra = jnp.concatenate(
        [
            total.reshape(every_rows, heads),
            kept(hi),
            kept(lo),
            jnp.zeros((every_rows, lanes - 3 * heads), jnp.float32),
        ],
        1,
    )
    scaled = weighted.reshape(heads, every_rows, head_dim)
    packed = jnp.concatenate([scaled, extra[None]], 0).astype(jnp.bfloat16)
    slots = packed.shape[0]
    packed = (
        packed.reshape(slots, n_wide, n_narrow, own, head_dim)
        .transpose(0, 2, 1, 3, 4)
        .reshape(slots, every_rows, head_dim)
    )
    packed = lax.psum_scatter(packed, "narrow", scatter_dimension=1, tiled=True)
    packed = lax.all_to_all(packed.reshape(slots, n_wide, own, head_dim), "wide", 1, 1)
    packed = packed.astype(jnp.float32)
    extra = packed[heads]
    part_shift = extra[..., heads : 2 * heads] + extra[..., 2 * heads : 3 * heads]
    part_scale = jnp.exp(part_shift - jnp.max(part_shift, 0)[None])
    total = jnp.sum(extra[..., :heads] * part_scale, 0)
    weighted = jnp.sum(packed[:heads] * part_scale.transpose(2, 0, 1)[..., None], 1)
    attended = weighted / total.T[..., None]
    attended = attended.astype(jnp.bfloat16).transpose(1, 0, 2).reshape(own, q_width)
    mine_rows = lax.all_gather(attended, "narrow", axis=0, tiled=True)
    mixed = tokens.astype(jnp.float32) + jnp.dot(
        mine_rows, w_out, preferred_element_type=jnp.float32
    )
    return mixed.astype(jnp.bfloat16)


def solution(mesh):
    return jax.shard_map(
        per_device,
        mesh=mesh,
        in_specs=(
            P(("rep", "wide"), "narrow"),
            P(),
            P(None, ("wide", "narrow")),
            P(None, "narrow"),
            P(None, "rep", ("wide", "narrow"), None, None),
            P(None, "rep", ("wide", "narrow"), None, None),
            P("rep"),
            P("rep"),
        ),
        out_specs=P(("rep", "wide"), "narrow"),
        check_vma=False,
    )
```

```python
import jax
import jax.numpy as jnp
from jax import lax
from jax.sharding import PartitionSpec as P

EPS = 1e-06
NEG = -1e30


def normalize(rows, gain):
    full = rows.astype(jnp.float32)
    meansq = jnp.mean(full * full, -1, keepdims=True)
    return (full * lax.rsqrt(meansq + EPS) * gain).astype(jnp.bfloat16)


def partial_softmax(grouped_queries, keys, values, allowed, form_s, form_o):
    scores = jnp.einsum(
        form_s, grouped_queries, keys, preferred_element_type=jnp.float32
    ) * grouped_queries.shape[-1] ** (-0.5)
    masked = jnp.where(allowed, scores, NEG)
    peak = jnp.max(masked, -1)
    weights = jnp.where(allowed, jnp.exp(masked - peak[..., None]), 0.0)
    total = jnp.sum(weights, -1)
    weighted = jnp.einsum(
        form_o, weights.astype(jnp.bfloat16), values, preferred_element_type=jnp.float32
    )
    return (peak, total, weighted)


def join_parts(first, second):
    peak = jnp.maximum(first[0], second[0])
    scale_a = jnp.exp(first[0] - peak)
    scale_b = jnp.exp(second[0] - peak)
    total = first[1] * scale_a + second[1] * scale_b
    weighted = first[2] * heads_major(scale_a) + second[2] * heads_major(scale_b)
    return (peak, total, weighted)


def heads_major(scale):
    return scale.transpose(1, 2, 0)[..., None]


def per_device(tokens, attn_gain, w_qkv, w_out, prefix_cache, decode_cache, offsets, lengths):
    n_wide = lax.axis_size("wide")
    n_narrow = lax.axis_size("narrow")
    devices = n_wide * n_narrow
    joined = lax.axis_index("wide") * n_narrow + lax.axis_index("narrow")
    block_rows = tokens.shape[0]
    every_rows = block_rows * n_wide
    own = every_rows // devices
    head_dim = prefix_cache.shape[-1]
    kv_heads = prefix_cache.shape[-2]
    n_prefix = prefix_cache.shape[1]
    n_decode = decode_cache.shape[1]
    span = (every_rows - n_decode) // n_prefix
    q_width = w_out.shape[0]
    heads = q_width // head_dim
    group = heads // kv_heads
    starts = (offsets[:, None] + jnp.arange(span, dtype=jnp.int32)[None, :]).reshape(-1)
    positions = jnp.concatenate([starts, lengths])
    row_ids = jnp.arange(every_rows, dtype=jnp.int32)
    sequence = jnp.where(
        row_ids < n_prefix * span, row_ids // span, row_ids - n_prefix * span + n_prefix
    )
    own_start = joined * own
    own_pos = lax.dynamic_slice_in_dim(positions, own_start, own)
    own_seq = lax.dynamic_slice_in_dim(sequence, own_start, own)
    features = lax.all_gather(tokens, "narrow", axis=1, tiled=True)
    normed_rows = normalize(features, attn_gain)
    w_cols = lax.all_gather(w_qkv, "wide", axis=0, tiled=False)
    part = jnp.einsum(
        "rf,wfc->rwc", normed_rows, w_cols, preferred_element_type=jnp.float32
    ).astype(jnp.bfloat16)
    col_block = w_qkv.shape[1]
    q_blocks = q_width // (n_narrow * col_block)
    gathered = lax.all_gather(part[:, :q_blocks], ("wide", "narrow"), axis=0, tiled=False)
    query_matrix = (
        gathered.reshape(n_wide, n_narrow, block_rows, q_blocks, col_block)
        .transpose(0, 2, 3, 1, 4)
        .reshape(every_rows, heads, head_dim)
    )
    fresh_kv = part[:, q_blocks:].reshape(n_narrow, own, col_block)
    fresh_kv = lax.all_to_all(fresh_kv, "narrow", 0, 0)
    own_keys = fresh_kv[:kv_heads].transpose(1, 0, 2)
    own_values = fresh_kv[kv_heads:].transpose(1, 0, 2)
    grouped_queries = query_matrix.reshape(every_rows, kv_heads, group, head_dim)
    shard = prefix_cache.shape[2]
    cache_pos = joined * shard + jnp.arange(shard, dtype=jnp.int32)
    pieces = []
    for index in range(n_prefix):
        block = grouped_queries[index * span : (index + 1) * span]
        allowed = (cache_pos < offsets[index])[None, None, None, :]
        pieces.append(
            partial_softmax(
                block,
                prefix_cache[0, index],
                prefix_cache[1, index],
                allowed,
                "qhgd,khd->qhgk",
                "qhgk,khd->hgqd",
            )
        )
    allowed = (cache_pos[None, :] < lengths[:, None])[:, None, None, :]
    pieces.append(
        partial_softmax(
            grouped_queries[n_prefix * span :],
            decode_cache[0],
            decode_cache[1],
            allowed,
            "nhgd,nkhd->nhgk",
            "nhgk,nkhd->hgnd",
        )
    )
    cached = tuple((jnp.concatenate([piece[slot] for piece in pieces], 2 * (slot // 2)) for slot in range(3)))
    allowed = ((sequence[:, None] == own_seq[None, :]) & (own_pos[None, :] <= positions[:, None]))[
        :, None, None, :
    ]
    fresh = partial_softmax(
        grouped_queries, own_keys, own_values, allowed, "rhgd,khd->rhgk", "rhgk,khd->hgrd"
    )
    peak, total, weighted = join_parts(cached, fresh)
    hi = lax.reduce_precision(peak, exponent_bits=8, mantissa_bits=7)
    lo = lax.reduce_precision(peak - hi, exponent_bits=8, mantissa_bits=7)
    scale = jnp.exp(jnp.minimum(peak - (hi + lo), 80.0))
    lanes = 128

    def slot(total, hi, lo):
        rows = total.shape[0]
        flat = lambda a: a.reshape(rows, heads)
        pad = jnp.zeros((rows, lanes - 3 * heads), jnp.float32)
        return jnp.concatenate([flat(total), flat(hi), flat(lo), pad], 1)

    scaled = (weighted * heads_major(scale)).reshape(heads, every_rows, head_dim)
    packed = jnp.concatenate([scaled, slot(total * scale, hi, lo)[None]], 0).astype(jnp.bfloat16)
    slots = packed.shape[0]
    packed = (
        packed.reshape(slots, n_wide, n_narrow, own, head_dim)
        .transpose(0, 2, 1, 3, 4)
        .reshape(slots, n_narrow, block_rows, head_dim)
    )
    packed = lax.all_to_all(packed, "narrow", 1, 1).astype(jnp.float32)
    extra = packed[heads]
    part_shift = extra[..., heads : 2 * heads] + extra[..., 2 * heads : 3 * heads]
    top = jnp.max(part_shift, 0)
    hi = lax.reduce_precision(top, exponent_bits=8, mantissa_bits=7)
    lo = lax.reduce_precision(top - hi, exponent_bits=8, mantissa_bits=7)
    part_scale = jnp.exp(jnp.minimum(part_shift - (hi + lo)[None], 80.0))
    total = jnp.sum(extra[..., :heads] * part_scale, 0)
    weighted = jnp.sum(packed[:heads] * part_scale.transpose(2, 0, 1)[..., None], 1)
    packed = jnp.concatenate([weighted, slot(total, hi, lo)[None]], 0).astype(jnp.bfloat16)
    packed = lax.all_to_all(packed.reshape(slots, n_wide, own, head_dim), "wide", 1, 1)
    packed = packed.astype(jnp.float32)
    extra = packed[heads]
    part_shift = extra[..., heads : 2 * heads] + extra[..., 2 * heads : 3 * heads]
    part_scale = jnp.exp(part_shift - jnp.max(part_shift, 0)[None])
    total = jnp.sum(extra[..., :heads] * part_scale, 0)
    weighted = jnp.sum(packed[:heads] * part_scale.transpose(2, 0, 1)[..., None], 1)
    attended = weighted / total.T[..., None]
    attended = attended.astype(jnp.bfloat16).transpose(1, 0, 2).reshape(own, q_width)
    mine_rows = lax.all_gather(attended, "narrow", axis=0, tiled=True)
    mixed = tokens.astype(jnp.float32) + jnp.dot(
        mine_rows, w_out, preferred_element_type=jnp.float32
    )
    return mixed.astype(jnp.bfloat16)


def solution(mesh):
    return jax.shard_map(
        per_device,
        mesh=mesh,
        in_specs=(
            P(("rep", "wide"), "narrow"),
            P(),
            P(None, ("wide", "narrow")),
            P(None, "narrow"),
            P(None, "rep", ("wide", "narrow"), None, None),
            P(None, "rep", ("wide", "narrow"), None, None),
            P("rep"),
            P("rep"),
        ),
        out_specs=P(("rep", "wide"), "narrow"),
        check_vma=False,
    )
```
